256 devices in a mesh: row: 16 (over x, z_hi, core), col: 4 (over y), rep: 4 (over z_lo).
Axes of the slice: x: 4, y: 4, z: 8 (z_hi: 2, z_lo: 4; z = z_hi * 4 + z_lo), core: 2. Of those that a mesh axis runs over, the one named last changes fastest.
Arguments:
- integrals: bfloat16 [8, 32, 60, 128, 128], P(None, 'row', 'rep', 'col'), may hold values from -0.0625 to 0.0625
- amplitudes: bfloat16 [8, 16, 60, 128, 128], P(None, 'col', 'rep', 'row'), may hold values from -6 to 6
- virt_count: int32 [8], replicated, may hold values from 76 to 128, as said below
- occ_irrep: int32 [60], replicated, may hold values from 0 to 7
Outputs:
- cycle: bfloat16 [8, 32, 128, 16, 128], P('rep', 'row', None, 'col')
The draws below stay inside these ranges and needn't reach their ends.
Inputs may be any that keep to these rules, and one draw needn't show every extreme that they name: `virt_count`: one irrep has exactly 128 virtual orbitals.
All inputs are finite; a program needn't handle non-finite values.
Results may differ from the reference program's by a relative error of at most 0.001.
Values may be sent and summed in bfloat16 or wider, within the bound.
No kernel may reach another device: no remote copies, remote signals or barrier semaphores. Data moves between devices by JAX's collectives and lax.ppermute only.
A program may use at most 128 MiB of HBM per device.

```python
import jax
import jax.numpy as jnp
from jax import lax

NG = 8
NVG = 128
NOCC = 60
OI = 32
OJ = 16


def draw_virt_count(key, part):
    lowest = NVG * 3 // 5
    counts = jax.random.randint(key, (NG,), lowest, NVG + 1)
    chosen = jax.random.randint(jax.random.fold_in(key, 7), (), 0, NG)
    return jnp.where(jnp.arange(NG) == chosen, NVG, counts).astype(jnp.int32)


def plant(result, own_key, least, high):
    spot = [jax.random.randint(jax.random.fold_in(own_key, axis), (), 0, length) for axis, length in enumerate(result.shape)]
    widest = result.shape.index(max(result.shape))
    beside = spot[:widest] + [(spot[widest] + 1) % result.shape[widest]] + spot[widest + 1:]
    return result.at[tuple(spot)].set(least).at[tuple(beside)].set(high)


def levels(rng, extent, shards, least, top_value):
    def one(axis_at, shards_of):
        draws = jax.random.uniform(jax.random.fold_in(jax.random.fold_in(rng, 6), axis_at), (shards_of,), jnp.float32, least / len(shards), top_value / len(shards))
        return jnp.repeat(jnp.exp(draws), extent[axis_at] // shards_of).reshape((-1,) + (1,) * (len(extent) - axis_at - 1))

    loudness = one(*shards[0])
    for cut in shards[1:]:
        loudness = loudness * one(*cut)
    return loudness


def bell_draw(key, extent, spread, most, pieces=(), held_as=jnp.bfloat16):
    values = jax.random.normal(key, extent, jnp.float32) * spread
    if len(pieces) > 0:
        values = levels(key, extent, pieces, -0.22, 0.18) * values
    return jnp.clip(values, min=-most, max=most).astype(held_as)


def setup_inputs(seed: int = 0) -> dict:
    seeds = jax.random.split(jax.random.key(seed), 5)
    return {
        "integrals": bell_draw(seeds[0], (NG, OI, NOCC, NVG, NVG), (NOCC * NVG) ** -0.5, 0.0625, ((1, 16), (2, 4), (3, 4))),
        "amplitudes": bell_draw(seeds[1], (NG, OJ, NOCC, NVG, NVG), 1.0, 6.0, ((1, 4), (2, 4), (3, 16))),
        "virt_count": draw_virt_count(jax.random.fold_in(seeds[4], 71), 0),
        "occ_irrep": plant(jax.random.randint(seeds[3], (NOCC,), 0, 8), jax.random.fold_in(seeds[3], 1), 0, 7).astype(jnp.int32),
    }


def reference(integrals, amplitudes, virt_count, occ_irrep):
    groups = jnp.arange(NG, dtype=jnp.int32)
    blocks = jnp.bitwise_xor(groups[:, None], occ_irrep[None, :].astype(jnp.int32))
    limit = virt_count[blocks]
    places = jnp.arange(NVG, dtype=jnp.int32)
    c_mask = places[None, None, :] < limit[:, :, None]
    a_mask = places[None, :] < virt_count[:, None]

    def one_block(items):
        weights, amps, alive, c_live = items
        keep = c_live[:, :, None] & alive[None, None, :]
        masked = jnp.where(keep[None], weights, jnp.zeros_like(weights))
        left = masked.astype(jnp.float32)
        right = amps.astype(jnp.float32)
        product = jnp.einsum("ikca,jkcb->iajb", left, right, precision=lax.Precision.HIGHEST)
        product = jnp.where(alive[None, None, None, :], product, jnp.zeros_like(product))
        return product.astype(jnp.bfloat16)

    return lax.map(one_block, (integrals, amplitudes, a_mask, c_mask))
```

```python
import jax
import jax.numpy as jnp
from jax import lax
from jax.sharding import PartitionSpec as P


def shift_perm(n, step, period=1):
    pairs = []
    for i in range(n):
        ring = n // period if period == 1 else 4
        pos = (i // period) % ring
        dest = i + ((pos + step) % ring - pos) * period
        pairs.append((i, dest))
    return pairs


def ring4_gather(block, axis, n, period, pos, split_axis):
    fwd = shift_perm(n, 1, period)
    bwd = shift_perm(n, -1, period)
    from_left = lax.ppermute(block, axis, fwd)
    from_right = lax.ppermute(block, axis, bwd)
    half = block.shape[split_axis] // 2
    lo = lax.slice_in_dim(from_left, 0, half, axis=split_axis)
    hi = lax.slice_in_dim(from_right, half, block.shape[split_axis], axis=split_axis)
    opp = jnp.concatenate(
        [lax.ppermute(lo, axis, fwd), lax.ppermute(hi, axis, bwd)], axis=split_axis
    )
    ring = jnp.stack([block, from_left, opp, from_right])
    return [lax.dynamic_index_in_dim(ring, (pos - q) % 4, 0, keepdims=False) for q in range(4)]


def gather_amplitudes(t_part):
    nrow = lax.axis_size("row")
    r = lax.axis_index("row")
    x = r // 4
    zh = (r // 2) % 2
    core = r % 2
    t_zh = lax.ppermute(t_part, "row", [(i, i ^ 2) for i in range(nrow)])
    pair = jnp.where(zh == 0, jnp.stack([t_part, t_zh]), jnp.stack([t_zh, t_part]))
    blocks = ring4_gather(pair, "row", nrow, 4, x, 1)
    mine = jnp.stack(blocks)
    other = lax.ppermute(mine, "row", [(i, i ^ 1) for i in range(nrow)])
    both = jnp.where(core == 0, jnp.stack([mine, other]), jnp.stack([other, mine]))
    ng, nj, nk, ncc, nb = t_part.shape
    full = jnp.transpose(both, (3, 4, 5, 1, 2, 0, 6, 7))
    return full.reshape(ng, nj, nk, 16 * ncc, nb)


def gather_integrals(w_part):
    ncol = lax.axis_size("col")
    cl = lax.axis_index("col")
    blocks = ring4_gather(w_part, "col", ncol, 1, cl, 0)
    return jnp.concatenate(blocks, axis=3)


def body(integrals, amplitudes, virt_count, occ_irrep):
    ngroup = integrals.shape[0]
    k_local = integrals.shape[2]
    c_local = integrals.shape[3]
    nvirt = integrals.shape[4]
    rep_index = lax.axis_index("rep")
    col_index = lax.axis_index("col")
    occ_local = lax.dynamic_slice_in_dim(occ_irrep, rep_index * k_local, k_local)
    groups = jnp.arange(ngroup, dtype=jnp.int32)
    blocks = jnp.bitwise_xor(groups[:, None], occ_local[None, :])
    onehot = blocks[:, :, None] == groups[None, None, :]
    limit = jnp.sum(jnp.where(onehot, virt_count[None, None, :], 0), axis=2)
    c_global = col_index * c_local + jnp.arange(c_local, dtype=jnp.int32)
    c_live = c_global[None, None, :] < limit[:, :, None]
    places = jnp.arange(nvirt, dtype=jnp.int32)
    a_live = places[None, :] < virt_count[:, None]
    keep = c_live[:, None, :, :, None] & a_live[:, None, None, None, :]
    masked = jnp.where(keep, integrals, jnp.zeros_like(integrals))
    owned = ngroup // lax.axis_size("rep")
    w_full = gather_integrals(masked)
    t_full = gather_amplitudes(amplitudes)
    partial_cycle = jnp.einsum(
        "gikca,gjkcb->giajb", w_full, t_full, preferred_element_type=jnp.float32
    )
    summed = lax.psum_scatter(partial_cycle, "rep", scatter_dimension=0, tiled=True)
    own_counts = lax.dynamic_slice_in_dim(virt_count, rep_index * owned, owned)
    b_live = places[None, :] < own_counts[:, None]
    result = jnp.where(b_live[:, None, None, None, :], summed, jnp.zeros_like(summed))
    return result.astype(jnp.bfloat16)


def solution(mesh):
    return jax.shard_map(
        body,
        mesh=mesh,
        in_specs=(P(None, "row", "rep", "col", None), P(None, "col", "rep", "row", None), P(), P()),
        out_specs=P("rep", "row", None, "col", None),
        check_vma=False,
    )
```

```python
import jax
import jax.numpy as jnp
from jax import lax
from jax.sharding import PartitionSpec as P


def shift_perm(n, step, period):
    pairs = []
    for i in range(n):
        pos = (i // period) % 4
        pairs.append((i, i + ((pos + step) % 4 - pos) * period))
    return pairs


def ring4_into(block, axis, n, period, pos, out_axis):
    fwd = shift_perm(n, 1, period)
    bwd = shift_perm(n, -1, period)
    from_left = lax.ppermute(block, axis, fwd)
    from_right = lax.ppermute(block, axis, bwd)
    half = block.shape[0] // 2
    opp_lo = lax.ppermute(from_left[:half], axis, fwd)
    opp_hi = lax.ppermute(from_right[half:], axis, bwd)
    width = block.shape[out_axis]
    shape = list(block.shape)
    shape[out_axis] = 4 * width
    opp = jnp.concatenate([opp_lo, opp_hi], axis=0)
    out = jnp.zeros(shape, block.dtype)
    for step, piece in enumerate([block, from_left, opp, from_right]):
        out = lax.dynamic_update_slice_in_dim(out, piece, ((pos - step) % 4) * width, axis=out_axis)
    return out


def gather_amplitudes(t_part):
    nrow = lax.axis_size("row")
    r = lax.axis_index("row")
    x = r // 4
    zh = (r // 2) % 2
    core = r % 2
    ng = t_part.shape[0]
    hg = ng // 2
    t_zh = lax.ppermute(t_part, "row", [(i, i ^ 2) for i in range(nrow)])
    pair = jnp.where(
        zh == 0, jnp.concatenate([t_part, t_zh], axis=3), jnp.concatenate([t_zh, t_part], axis=3)
    )
    keep = jnp.where(core == 0, pair[:hg], pair[hg:])
    send = jnp.where(core == 0, pair[hg:], pair[:hg])
    got = lax.ppermute(send, "row", [(i, i ^ 1) for i in range(nrow)])
    quad = jnp.where(
        core == 0, jnp.concatenate([keep, got], axis=3), jnp.concatenate([got, keep], axis=3)
    )
    mine = ring4_into(quad, "row", nrow, 4, x, 3)
    other = lax.ppermute(mine, "row", [(i, i ^ 1) for i in range(nrow)])
    shape = list(mine.shape)
    shape[0] = ng
    full = jnp.zeros(shape, mine.dtype)
    full = lax.dynamic_update_slice_in_dim(full, mine, core * hg, axis=0)
    full = lax.dynamic_update_slice_in_dim(full, other, (1 - core) * hg, axis=0)
    return full


def gather_integrals(w_part):
    ng, ni, nk, nc, na = w_part.shape
    w = w_part.reshape(ng, ni, nk, 2, 2, nc // 4, na)
    w = jnp.transpose(w, (0, 1, 2, 4, 3, 5, 6)).reshape(ng, ni, nk, nc, na)
    ncol = lax.axis_size("col")
    cl = lax.axis_index("col")
    return ring4_into(w, "col", ncol, 1, cl, 3)


def body(integrals, amplitudes, virt_count, occ_irrep):
    ngroup = integrals.shape[0]
    k_local = integrals.shape[2]
    c_local = integrals.shape[3]
    nvirt = integrals.shape[4]
    rep_index = lax.axis_index("rep")
    col_index = lax.axis_index("col")
    occ_local = lax.dynamic_slice_in_dim(occ_irrep, rep_index * k_local, k_local)
    groups = jnp.arange(ngroup, dtype=jnp.int32)
    blocks = jnp.bitwise_xor(groups[:, None], occ_local[None, :])
    onehot = blocks[:, :, None] == groups[None, None, :]
    limit = jnp.sum(jnp.where(onehot, virt_count[None, None, :], 0), axis=2)
    c_global = col_index * c_local + jnp.arange(c_local, dtype=jnp.int32)
    c_live = c_global[None, None, :] < limit[:, :, None]
    places = jnp.arange(nvirt, dtype=jnp.int32)
    a_live = places[None, :] < virt_count[:, None]
    keep = c_live[:, None, :, :, None] & a_live[:, None, None, None, :]
    masked = jnp.where(keep, integrals, jnp.zeros_like(integrals))
    owned = ngroup // lax.axis_size("rep")
    w_full = gather_integrals(masked)
    t_full = gather_amplitudes(amplitudes)
    partial_cycle = jnp.einsum(
        "gikca,gjkcb->giajb", w_full, t_full, preferred_element_type=jnp.float32
    )
    summed = lax.psum_scatter(partial_cycle, "rep", scatter_dimension=0, tiled=True)
    own_counts = lax.dynamic_slice_in_dim(virt_count, rep_index * owned, owned)
    b_live = places[None, :] < own_counts[:, None]
    result = jnp.where(b_live[:, None, None, None, :], summed, jnp.zeros_like(summed))
    return result.astype(jnp.bfloat16)


def solution(mesh):
    return jax.shard_map(
        body,
        mesh=mesh,
        in_specs=(P(None, "row", "rep", "col", None), P(None, "col", "rep", "row", None), P(), P()),
        out_specs=P("rep", "row", None, "col", None),
        check_vma=False,
    )
```

```python
import jax
import jax.numpy as jnp
from jax import lax
from jax.sharding import PartitionSpec as P


def shift_perm(n, step, period):
    pairs = []
    for i in range(n):
        pos = (i // period) % 4
        pairs.append((i, i + ((pos + step) % 4 - pos) * period))
    return pairs


def ring4_into(block, axis, n, period, pos, out_axis):
    fwd = shift_perm(n, 1, period)
    bwd = shift_perm(n, -1, period)
    from_left = lax.ppermute(block, axis, fwd)
    from_right = lax.ppermute(block, axis, bwd)
    half = block.shape[0] // 2
    opp_lo = lax.ppermute(from_left[:half], axis, fwd)
    opp_hi = lax.ppermute(from_right[half:], axis, bwd)
    width = block.shape[out_axis]
    shape = list(block.shape)
    shape[out_axis] = 4 * width
    opp = jnp.concatenate([opp_lo, opp_hi], axis=0)
    out = jnp.zeros(shape, block.dtype)
    for step, piece in enumerate([block, from_left, opp, from_right]):
        out = lax.dynamic_update_slice_in_dim(out, piece, ((pos - step) % 4) * width, axis=out_axis)
    return out


def gather_amplitudes(t_part, cl):
    nrow = lax.axis_size("row")
    r = lax.axis_index("row")
    x = r // 4
    zh = (r // 2) % 2
    core = r % 2
    hj = t_part.shape[1] // 2
    t_zh = lax.ppermute(t_part, "row", [(i, i ^ 2) for i in range(nrow)])
    pair = jnp.where(
        zh == 0, jnp.concatenate([t_part, t_zh], axis=3), jnp.concatenate([t_zh, t_part], axis=3)
    )
    keep = jnp.where(core == 0, pair[:, :hj], pair[:, hj:])
    send = jnp.where(core == 0, pair[:, hj:], pair[:, :hj])
    got = lax.ppermute(send, "row", [(i, i ^ 1) for i in range(nrow)])
    quad = jnp.where(
        core == 0, jnp.concatenate([keep, got], axis=3), jnp.concatenate([got, keep], axis=3)
    )
    mine = ring4_into(quad, "row", nrow, 4, x - cl, 3)
    other = lax.ppermute(mine, "row", [(i, i ^ 1) for i in range(nrow)])
    return mine, other


def gather_integrals(w_part):
    ng, ni, nk, nc, na = w_part.shape
    w = w_part.reshape(ng, ni, nk, 2, 2, nc // 4, na)
    w = jnp.transpose(w, (0, 1, 2, 6, 4, 3, 5)).reshape(ng, ni, nk, na, nc)
    fwd = shift_perm(4, 1, 1)
    bwd = shift_perm(4, -1, 1)
    from_left = lax.ppermute(w, "col", fwd)
    from_right = lax.ppermute(w, "col", bwd)
    half = ng // 2
    opp_lo = lax.ppermute(from_left[:half], "col", fwd)
    opp_hi = lax.ppermute(from_right[half:], "col", bwd)
    opp = jnp.concatenate([opp_lo, opp_hi], axis=0)
    return jnp.concatenate([w, from_right, opp, from_left], axis=4)


def body(integrals, amplitudes, virt_count, occ_irrep):
    ngroup = integrals.shape[0]
    k_local = integrals.shape[2]
    c_local = integrals.shape[3]
    nvirt = integrals.shape[4]
    rep_index = lax.axis_index("rep")
    col_index = lax.axis_index("col")
    core = lax.axis_index("row") % 2
    occ_local = lax.dynamic_slice_in_dim(occ_irrep, rep_index * k_local, k_local)
    groups = jnp.arange(ngroup, dtype=jnp.int32)
    blocks = jnp.bitwise_xor(groups[:, None], occ_local[None, :])
    onehot = blocks[:, :, None] == groups[None, None, :]
    limit = jnp.sum(jnp.where(onehot, virt_count[None, None, :], 0), axis=2)
    c_global = col_index * c_local + jnp.arange(c_local, dtype=jnp.int32)
    c_live = c_global[None, None, :] < limit[:, :, None]
    places = jnp.arange(nvirt, dtype=jnp.int32)
    a_live = places[None, :] < virt_count[:, None]
    keep = c_live[:, None, :, :, None] & a_live[:, None, None, None, :]
    masked = jnp.where(keep, integrals, jnp.zeros_like(integrals))
    owned = ngroup // lax.axis_size("rep")
    w_full = gather_integrals(masked)
    t_mine, t_other = gather_amplitudes(amplitudes, col_index)
    sums = []
    for t_half in (t_mine, t_other):
        part = jnp.einsum("gikac,gjkcb->giajb", w_full, t_half, preferred_element_type=jnp.float32)
        sums.append(lax.psum_scatter(part, "rep", scatter_dimension=0, tiled=True))
    summed = jnp.where(
        core == 0, jnp.concatenate(sums, axis=3), jnp.concatenate(sums[::-1], axis=3)
    )
    own_counts = lax.dynamic_slice_in_dim(virt_count, rep_index * owned, owned)
    b_live = places[None, :] < own_counts[:, None]
    result = jnp.where(b_live[:, None, None, None, :], summed, jnp.zeros_like(summed))
    return result.astype(jnp.bfloat16)


def solution(mesh):
    return jax.shard_map(
        body,
        mesh=mesh,
        in_specs=(P(None, "row", "rep", "col", None), P(None, "col", "rep", "row", None), P(), P()),
        out_specs=P("rep", "row", None, "col", None),
        check_vma=False,
    )
```

```python
import jax
import jax.numpy as jnp
from jax import lax
from jax.sharding import PartitionSpec as P


def shift_perm(n, step, period):
    pairs = []
    for i in range(n):
        pos = (i // period) % 4
        pairs.append((i, i + ((pos + step) % 4 - pos) * period))
    return pairs


def ring4_into(block, axis, n, period, pos, out_axis):
    fwd = shift_perm(n, 1, period)
    bwd = shift_perm(n, -1, period)
    from_left = lax.ppermute(block, axis, fwd)
    from_right = lax.ppermute(block, axis, bwd)
    half = block.shape[0] // 2
    opp_lo = lax.ppermute(from_left[:half], axis, fwd)
    opp_hi = lax.ppermute(from_right[half:], axis, bwd)
    width = block.shape[out_axis]
    shape = list(block.shape)
    shape[out_axis] = 4 * width
    opp = jnp.concatenate([opp_lo, opp_hi], axis=0)
    out = jnp.zeros(shape, block.dtype)
    for step, piece in enumerate([block, from_left, opp, from_right]):
        out = lax.dynamic_update_slice_in_dim(out, piece, ((pos - step) % 4) * width, axis=out_axis)
    return out


def gather_amplitudes(t_part, cl):
    nrow = lax.axis_size("row")
    r = lax.axis_index("row")
    x = r // 4
    zh = (r // 2) % 2
    core = r % 2
    hj = t_part.shape[1] // 2
    t_zh = lax.ppermute(t_part, "row", [(i, i ^ 2) for i in range(nrow)])
    pair = jnp.where(
        zh == 0, jnp.concatenate([t_part, t_zh], axis=3), jnp.concatenate([t_zh, t_part], axis=3)
    )
    keep = jnp.where(core == 0, pair[:, :hj], pair[:, hj:])
    send = jnp.where(core == 0, pair[:, hj:], pair[:, :hj])
    got = lax.ppermute(send, "row", [(i, i ^ 1) for i in range(nrow)])
    ng, nh, nk, nzc, nb = keep.shape
    keep5 = keep.reshape(ng, nh, nk, 2, nzc // 2, nb)
    got5 = got.reshape(ng, nh, nk, 2, nzc // 2, nb)
    quad = jnp.where(
        core == 0, jnp.stack([keep5, got5], axis=4), jnp.stack([got5, keep5], axis=4)
    ).reshape(ng, nh, nk, 2 * nzc, nb)
    mine = ring4_into(quad, "row", nrow, 4, x - cl, 3)
    other = lax.ppermute(mine, "row", [(i, i ^ 1) for i in range(nrow)])
    return mine, other


def gather_integrals(w_part):
    ng = w_part.shape[0]
    w = w_part
    fwd = shift_perm(4, 1, 1)
    bwd = shift_perm(4, -1, 1)
    from_left = lax.ppermute(w, "col", fwd)
    from_right = lax.ppermute(w, "col", bwd)
    half = ng // 2
    opp_lo = lax.ppermute(from_left[:half], "col", fwd)
    opp_hi = lax.ppermute(from_right[half:], "col", bwd)
    opp = jnp.concatenate([opp_lo, opp_hi], axis=0)
    return [w, from_right, opp, from_left]


def body(integrals, amplitudes, virt_count, occ_irrep):
    ngroup = integrals.shape[0]
    k_local = integrals.shape[2]
    c_local = integrals.shape[3]
    nvirt = integrals.shape[4]
    rep_index = lax.axis_index("rep")
    col_index = lax.axis_index("col")
    core = lax.axis_index("row") % 2
    occ_local = lax.dynamic_slice_in_dim(occ_irrep, rep_index * k_local, k_local)
    groups = jnp.arange(ngroup, dtype=jnp.int32)
    blocks = jnp.bitwise_xor(groups[:, None], occ_local[None, :])
    onehot = blocks[:, :, None] == groups[None, None, :]
    limit = jnp.sum(jnp.where(onehot, virt_count[None, None, :], 0), axis=2)
    c_global = col_index * c_local + jnp.arange(c_local, dtype=jnp.int32)
    c_live = c_global[None, None, :] < limit[:, :, None]
    places = jnp.arange(nvirt, dtype=jnp.int32)
    a_live = places[None, :] < virt_count[:, None]
    keep = c_live[:, None, :, :, None] & a_live[:, None, None, None, :]
    masked = jnp.where(keep, integrals, jnp.zeros_like(integrals))
    owned = ngroup // lax.axis_size("rep")
    w_blocks = gather_integrals(masked)
    t_mine, t_other = gather_amplitudes(amplitudes, col_index)
    sums = []
    for t_half in (t_mine, t_other):
        width = c_local
        part = None
        for s, w_blk in enumerate(w_blocks):
            term = jnp.einsum(
                "gikca,gjkcb->giajb",
                w_blk,
                t_half[:, :, :, s * width:(s + 1) * width],
                preferred_element_type=jnp.float32,
            )
            part = term if part is None else part + term
        sums.append(lax.psum_scatter(part, "rep", scatter_dimension=0, tiled=True))
    summed = jnp.where(
        core == 0, jnp.concatenate(sums, axis=3), jnp.concatenate(sums[::-1], axis=3)
    )
    own_counts = lax.dynamic_slice_in_dim(virt_count, rep_index * owned, owned)
    b_live = places[None, :] < own_counts[:, None]
    result = jnp.where(b_live[:, None, None, None, :], summed, jnp.zeros_like(summed))
    return result.astype(jnp.bfloat16)


def solution(mesh):
    return jax.shard_map(
        body,
        mesh=mesh,
        in_specs=(P(None, "row", "rep", "col", None), P(None, "col", "rep", "row", None), P(), P()),
        out_specs=P("rep", "row", None, "col", None),
        check_vma=False,
    )
```

```python
import jax
import jax.numpy as jnp
from jax import lax
from jax.sharding import PartitionSpec as P


def shift_perm(n, step, period):
    pairs = []
    for i in range(n):
        pos = (i // period) % 4
        pairs.append((i, i + ((pos + step) % 4 - pos) * period))
    return pairs


def ring4_pieces(block, axis, n, period):
    fwd = shift_perm(n, 1, period)
    bwd = shift_perm(n, -1, period)
    from_left = lax.ppermute(block, axis, fwd)
    from_right = lax.ppermute(block, axis, bwd)
    half = block.shape[0] // 2
    opp_lo = lax.ppermute(from_left[:half], axis, fwd)
    opp_hi = lax.ppermute(from_right[half:], axis, bwd)
    opp = jnp.concatenate([opp_lo, opp_hi], axis=0)
    return [block, from_left, opp, from_right]


def core_quad(part, core, nrow, hj):
    keep = jnp.where(core == 0, part[:, :hj], part[:, hj:])
    send = jnp.where(core == 0, part[:, hj:], part[:, :hj])
    got = lax.ppermute(send, "row", [(i, i ^ 1) for i in range(nrow)])
    return jnp.where(
        core == 0, jnp.concatenate([keep, got], axis=3), jnp.concatenate([got, keep], axis=3)
    )


def gather_amplitudes(t_part, cl):
    nrow = lax.axis_size("row")
    r = lax.axis_index("row")
    x = r // 4
    zh = (r // 2) % 2
    core = r % 2
    ng, nj, nk, ncc, nb = t_part.shape
    hj = nj // 2
    t_zh = lax.ppermute(t_part, "row", [(i, i ^ 2) for i in range(nrow)])
    own = ring4_pieces(core_quad(t_part, core, nrow, hj), "row", nrow, 4)
    pos = x - cl
    mine = jnp.zeros((ng, hj, nk, 16 * ncc, nb), t_part.dtype)
    for step, piece in enumerate(own):
        mine = lax.dynamic_update_slice_in_dim(
            mine, piece, ((pos - step) % 4) * 4 * ncc + zh * 2 * ncc, axis=3
        )
    far = ring4_pieces(core_quad(t_zh, core, nrow, hj), "row", nrow, 4)
    for step, piece in enumerate(far):
        mine = lax.dynamic_update_slice_in_dim(
            mine, piece, ((pos - step) % 4) * 4 * ncc + (1 - zh) * 2 * ncc, axis=3
        )
    other = lax.ppermute(mine, "row", [(i, i ^ 1) for i in range(nrow)])
    return mine, other


def gather_integrals(w_part):
    ng = w_part.shape[0]
    w = w_part
    fwd = shift_perm(4, 1, 1)
    bwd = shift_perm(4, -1, 1)
    from_left = lax.ppermute(w, "col", fwd)
    from_right = lax.ppermute(w, "col", bwd)
    half = ng // 2
    opp_lo = lax.ppermute(from_left[:half], "col", fwd)
    opp_hi = lax.ppermute(from_right[half:], "col", bwd)
    opp = jnp.concatenate([opp_lo, opp_hi], axis=0)
    return [w, from_right, opp, from_left]


def body(integrals, amplitudes, virt_count, occ_irrep):
    ngroup = integrals.shape[0]
    k_local = integrals.shape[2]
    c_local = integrals.shape[3]
    nvirt = integrals.shape[4]
    rep_index = lax.axis_index("rep")
    col_index = lax.axis_index("col")
    core = lax.axis_index("row") % 2
    occ_local = lax.dynamic_slice_in_dim(occ_irrep, rep_index * k_local, k_local)
    groups = jnp.arange(ngroup, dtype=jnp.int32)
    blocks = jnp.bitwise_xor(groups[:, None], occ_local[None, :])
    onehot = blocks[:, :, None] == groups[None, None, :]
    limit = jnp.sum(jnp.where(onehot, virt_count[None, None, :], 0), axis=2)
    c_global = col_index * c_local + jnp.arange(c_local, dtype=jnp.int32)
    c_live = c_global[None, None, :] < limit[:, :, None]
    places = jnp.arange(nvirt, dtype=jnp.int32)
    a_live = places[None, :] < virt_count[:, None]
    keep = c_live[:, None, :, :, None] & a_live[:, None, None, None, :]
    masked = jnp.where(keep, integrals, jnp.zeros_like(integrals))
    owned = ngroup // lax.axis_size("rep")
    w_blocks = gather_integrals(masked)
    t_mine, t_other = gather_amplitudes(amplitudes, col_index)
    sums = []
    for t_half in (t_mine, t_other):
        width = c_local
        part = None
        for s, w_blk in enumerate(w_blocks):
            term = jnp.einsum(
                "gikca,gjkcb->giajb",
                w_blk,
                t_half[:, :, :, s * width:(s + 1) * width],
                preferred_element_type=jnp.float32,
            )
            part = term if part is None else part + term
        sums.append(lax.psum_scatter(part, "rep", scatter_dimension=0, tiled=True))
    summed = jnp.where(
        core == 0, jnp.concatenate(sums, axis=3), jnp.concatenate(sums[::-1], axis=3)
    )
    own_counts = lax.dynamic_slice_in_dim(virt_count, rep_index * owned, owned)
    b_live = places[None, :] < own_counts[:, None]
    result = jnp.where(b_live[:, None, None, None, :], summed, jnp.zeros_like(summed))
    return result.astype(jnp.bfloat16)


def solution(mesh):
    return jax.shard_map(
        body,
        mesh=mesh,
        in_specs=(P(None, "row", "rep", "col", None), P(None, "col", "rep", "row", None), P(), P()),
        out_specs=P("rep", "row", None, "col", None),
        check_vma=False,
    )
```

```python
import jax
import jax.numpy as jnp
from jax import lax
from jax.sharding import PartitionSpec as P


def shift_perm(n, step, period):
    pairs = []
    for i in range(n):
        pos = (i // period) % 4
        pairs.append((i, i + ((pos + step) % 4 - pos) * period))
    return pairs


def ring4_pieces(block, axis, n, period):
    fwd = shift_perm(n, 1, period)
    bwd = shift_perm(n, -1, period)
    from_left = lax.ppermute(block, axis, fwd)
    from_right = lax.ppermute(block, axis, bwd)
    half = block.shape[0] // 2
    opp_lo = lax.ppermute(from_left[:half], axis, fwd)
    opp_hi = lax.ppermute(from_right[half:], axis, bwd)
    opp = jnp.concatenate([opp_lo, opp_hi], axis=0)
    return [block, from_left, opp, from_right]


def core_quad(part, core, nrow, hj):
    keep = jnp.where(core == 0, part[:, :hj], part[:, hj:])
    send = jnp.where(core == 0, part[:, hj:], part[:, :hj])
    got = lax.ppermute(send, "row", [(i, i ^ 1) for i in range(nrow)])
    return jnp.where(
        core == 0, jnp.concatenate([keep, got], axis=3), jnp.concatenate([got, keep], axis=3)
    )


def gather_amplitudes(t_part, cl):
    nrow = lax.axis_size("row")
    r = lax.axis_index("row")
    x = r // 4
    zh = (r // 2) % 2
    core = r % 2
    ng, nj, nk, ncc, nb = t_part.shape
    hj = nj // 2
    t_zh = lax.ppermute(t_part, "row", [(i, i ^ 2) for i in range(nrow)])
    own = ring4_pieces(core_quad(t_part, core, nrow, hj), "row", nrow, 4)
    pos = x - cl
    mine = jnp.zeros((ng, hj, nk, 16 * ncc, nb), t_part.dtype)
    for step, piece in enumerate(own):
        mine = lax.dynamic_update_slice_in_dim(
            mine, piece, ((pos - step) % 4) * 4 * ncc + zh * 2 * ncc, axis=3
        )
    far = ring4_pieces(core_quad(t_zh, core, nrow, hj), "row", nrow, 4)
    for step, piece in enumerate(far):
        mine = lax.dynamic_update_slice_in_dim(
            mine, piece, ((pos - step) % 4) * 4 * ncc + (1 - zh) * 2 * ncc, axis=3
        )
    other = lax.ppermute(mine, "row", [(i, i ^ 1) for i in range(nrow)])
    return mine, other


def gather_integrals(w_part):
    ng = w_part.shape[0]
    w = w_part
    fwd = shift_perm(4, 1, 1)
    bwd = shift_perm(4, -1, 1)
    from_left = lax.ppermute(w, "col", fwd)
    from_right = lax.ppermute(w, "col", bwd)
    half = ng // 2
    opp_lo = lax.ppermute(from_left[:half], "col", fwd)
    opp_hi = lax.ppermute(from_right[half:], "col", bwd)
    opp = jnp.concatenate([opp_lo, opp_hi], axis=0)
    return [w, from_right, opp, from_left]


def ring_reduce_scatter(part):
    n = lax.axis_size("rep")
    d = lax.axis_index("rep")
    width = part.shape[0] // n
    fwd = [(i, (i + 1) % n) for i in range(n)]

    def chunk(t):
        return lax.dynamic_slice_in_dim(part, (t % n) * width, width, axis=0)

    acc = chunk(d + n - 1)
    for step in range(1, n):
        acc = lax.ppermute(acc, "rep", fwd) + chunk(d + 2 * n - step - 1)
    return acc


def body(integrals, amplitudes, virt_count, occ_irrep):
    ngroup = integrals.shape[0]
    k_local = integrals.shape[2]
    c_local = integrals.shape[3]
    nvirt = integrals.shape[4]
    rep_index = lax.axis_index("rep")
    col_index = lax.axis_index("col")
    core = lax.axis_index("row") % 2
    occ_local = lax.dynamic_slice_in_dim(occ_irrep, rep_index * k_local, k_local)
    groups = jnp.arange(ngroup, dtype=jnp.int32)
    blocks = jnp.bitwise_xor(groups[:, None], occ_local[None, :])
    onehot = blocks[:, :, None] == groups[None, None, :]
    limit = jnp.sum(jnp.where(onehot, virt_count[None, None, :], 0), axis=2)
    c_global = col_index * c_local + jnp.arange(c_local, dtype=jnp.int32)
    c_live = c_global[None, None, :] < limit[:, :, None]
    places = jnp.arange(nvirt, dtype=jnp.int32)
    a_live = places[None, :] < virt_count[:, None]
    keep = c_live[:, None, :, :, None] & a_live[:, None, None, None, :]
    masked = jnp.where(keep, integrals, jnp.zeros_like(integrals))
    owned = ngroup // lax.axis_size("rep")
    w_blocks = gather_integrals(masked)
    t_mine, t_other = gather_amplitudes(amplitudes, col_index)
    sums = []
    for t_half, name in ((t_mine, "em"), (t_other, "eo")):
        width = c_local
        part = None
        for s, w_blk in enumerate(w_blocks):
            term = jnp.einsum(
                "gikca,gjkcb->giajb",
                w_blk,
                t_half[:, :, :, s * width:(s + 1) * width],
                preferred_element_type=jnp.float32,
            )
            part = term if part is None else part + term
        if name == "em":
            sums.append(ring_reduce_scatter(part))
        else:
            sums.append(lax.psum_scatter(part, "rep", scatter_dimension=0, tiled=True))
    summed = jnp.where(
        core == 0, jnp.concatenate(sums, axis=3), jnp.concatenate(sums[::-1], axis=3)
    )
    own_counts = lax.dynamic_slice_in_dim(virt_count, rep_index * owned, owned)
    b_live = places[None, :] < own_counts[:, None]
    result = jnp.where(b_live[:, None, None, None, :], summed, jnp.zeros_like(summed))
    return result.astype(jnp.bfloat16)


def solution(mesh):
    return jax.shard_map(
        body,
        mesh=mesh,
        in_specs=(P(None, "row", "rep", "col", None), P(None, "col", "rep", "row", None), P(), P()),
        out_specs=P("rep", "row", None, "col", None),
        check_vma=False,
    )
```

```python
import jax
import jax.numpy as jnp
from jax import lax
from jax.sharding import PartitionSpec as P


def shift_perm(n, step, period):
    pairs = []
    for i in range(n):
        pos = (i // period) % 4
        pairs.append((i, i + ((pos + step) % 4 - pos) * period))
    return pairs


def ring4_pieces(block, axis, n, period):
    fwd = shift_perm(n, 1, period)
    bwd = shift_perm(n, -1, period)
    from_left = lax.ppermute(block, axis, fwd)
    from_right = lax.ppermute(block, axis, bwd)
    half = block.shape[0] // 2
    opp_lo = lax.ppermute(from_left[:half], axis, fwd)
    opp_hi = lax.ppermute(from_right[half:], axis, bwd)
    opp = jnp.concatenate([opp_lo, opp_hi], axis=0)
    return [block, from_left, opp, from_right]


def core_quad(part, core, nrow, hj):
    keep = jnp.where(core == 0, part[:, :hj], part[:, hj:])
    send = jnp.where(core == 0, part[:, hj:], part[:, :hj])
    got = lax.ppermute(send, "row", [(i, i ^ 1) for i in range(nrow)])
    return jnp.where(
        core == 0, jnp.concatenate([keep, got], axis=3), jnp.concatenate([got, keep], axis=3)
    )


def z_shift_perm(nrow, nrep, step):
    pairs = []
    for r in range(nrow):
        zh = (r >> 1) & 1
        for zl in range(nrep):
            z = (zh * nrep + zl + step) % (2 * nrep)
            dst_row = (r & ~2) | ((z // nrep) << 1)
            pairs.append((r * nrep + zl, dst_row * nrep + z % nrep))
    return pairs


def zh_swap(part, nrow):
    nrep = lax.axis_size("rep")
    plus = z_shift_perm(nrow, nrep, 2)
    minus = z_shift_perm(nrow, nrep, -2)
    half = part.shape[0] // 2
    lo = part[:half]
    hi = part[half:]
    lo = lax.ppermute(lo, ("row", "rep"), plus)
    hi = lax.ppermute(hi, ("row", "rep"), minus)
    lo = lax.ppermute(lo, ("row", "rep"), plus)
    hi = lax.ppermute(hi, ("row", "rep"), minus)
    return jnp.concatenate([lo, hi], axis=0)


def gather_amplitudes(t_part, cl):
    nrow = lax.axis_size("row")
    r = lax.axis_index("row")
    x = r // 4
    zh = (r // 2) % 2
    core = r % 2
    ng, nj, nk, ncc, nb = t_part.shape
    hj = nj // 2
    t_zh = zh_swap(t_part, nrow)
    own = ring4_pieces(core_quad(t_part, core, nrow, hj), "row", nrow, 4)
    pos = x - cl
    mine = jnp.zeros((ng, hj, nk, 16 * ncc, nb), t_part.dtype)
    for step, piece in enumerate(own):
        mine = lax.dynamic_update_slice_in_dim(
            mine, piece, ((pos - step) % 4) * 4 * ncc + zh * 2 * ncc, axis=3
        )
    far = ring4_pieces(core_quad(t_zh, core, nrow, hj), "row", nrow, 4)
    for step, piece in enumerate(far):
        mine = lax.dynamic_update_slice_in_dim(
            mine, piece, ((pos - step) % 4) * 4 * ncc + (1 - zh) * 2 * ncc, axis=3
        )
    other = lax.ppermute(mine, "row", [(i, i ^ 1) for i in range(nrow)])
    return mine, other


def gather_integrals(w_part):
    ng = w_part.shape[0]
    w = w_part
    fwd = shift_perm(4, 1, 1)
    bwd = shift_perm(4, -1, 1)
    from_left = lax.ppermute(w, "col", fwd)
    from_right = lax.ppermute(w, "col", bwd)
    half = ng // 2
    opp_lo = lax.ppermute(from_left[:half], "col", fwd)
    opp_hi = lax.ppermute(from_right[half:], "col", bwd)
    opp = jnp.concatenate([opp_lo, opp_hi], axis=0)
    return [w, from_right, opp, from_left]


def ring_reduce_scatter(part):
    n = lax.axis_size("rep")
    d = lax.axis_index("rep")
    width = part.shape[0] // n
    fwd = [(i, (i + 1) % n) for i in range(n)]

    def chunk(t):
        return lax.dynamic_slice_in_dim(part, (t % n) * width, width, axis=0)

    acc = chunk(d + n - 1)
    for step in range(1, n):
        acc = lax.ppermute(acc, "rep", fwd) + chunk(d + 2 * n - step - 1)
    return acc


def body(integrals, amplitudes, virt_count, occ_irrep):
    ngroup = integrals.shape[0]
    k_local = integrals.shape[2]
    c_local = integrals.shape[3]
    nvirt = integrals.shape[4]
    rep_index = lax.axis_index("rep")
    col_index = lax.axis_index("col")
    core = lax.axis_index("row") % 2
    occ_local = lax.dynamic_slice_in_dim(occ_irrep, rep_index * k_local, k_local)
    groups = jnp.arange(ngroup, dtype=jnp.int32)
    blocks = jnp.bitwise_xor(groups[:, None], occ_local[None, :])
    onehot = blocks[:, :, None] == groups[None, None, :]
    limit = jnp.sum(jnp.where(onehot, virt_count[None, None, :], 0), axis=2)
    c_global = col_index * c_local + jnp.arange(c_local, dtype=jnp.int32)
    c_live = c_global[None, None, :] < limit[:, :, None]
    places = jnp.arange(nvirt, dtype=jnp.int32)
    a_live = places[None, :] < virt_count[:, None]
    keep = c_live[:, None, :, :, None] & a_live[:, None, None, None, :]
    masked = jnp.where(keep, integrals, jnp.zeros_like(integrals))
    owned = ngroup // lax.axis_size("rep")
    w_blocks = gather_integrals(masked)
    t_mine, t_other = gather_amplitudes(amplitudes, col_index)
    sums = []
    for t_half, name in ((t_mine, "em"), (t_other, "eo")):
        width = c_local
        part = None
        for s, w_blk in enumerate(w_blocks):
            term = jnp.einsum(
                "gikca,gjkcb->giajb",
                w_blk,
                t_half[:, :, :, s * width:(s + 1) * width],
                preferred_element_type=jnp.float32,
            )
            part = term if part is None else part + term
        if name == "em":
            sums.append(ring_reduce_scatter(part))
        else:
            sums.append(lax.psum_scatter(part, "rep", scatter_dimension=0, tiled=True))
    summed = jnp.where(
        core == 0, jnp.concatenate(sums, axis=3), jnp.concatenate(sums[::-1], axis=3)
    )
    own_counts = lax.dynamic_slice_in_dim(virt_count, rep_index * owned, owned)
    b_live = places[None, :] < own_counts[:, None]
    result = jnp.where(b_live[:, None, None, None, :], summed, jnp.zeros_like(summed))
    return result.astype(jnp.bfloat16)


def solution(mesh):
    return jax.shard_map(
        body,
        mesh=mesh,
        in_specs=(P(None, "row", "rep", "col", None), P(None, "col", "rep", "row", None), P(), P()),
        out_specs=P("rep", "row", None, "col", None),
        check_vma=False,
    )
```

```python
import jax
import jax.numpy as jnp
from jax import lax
from jax.sharding import PartitionSpec as P


def shift_perm(n, step, period):
    pairs = []
    for i in range(n):
        pos = (i // period) % 4
        pairs.append((i, i + ((pos + step) % 4 - pos) * period))
    return pairs


def ring4_pieces(block, axis, n, period):
    fwd = shift_perm(n, 1, period)
    bwd = shift_perm(n, -1, period)
    from_left = lax.ppermute(block, axis, fwd)
    from_right = lax.ppermute(block, axis, bwd)
    half = block.shape[0] // 2
    opp_lo = lax.ppermute(from_left[:half], axis, fwd)
    opp_hi = lax.ppermute(from_right[half:], axis, bwd)
    opp = jnp.concatenate([opp_lo, opp_hi], axis=0)
    return [block, from_left, opp, from_right]


def core_quad(part, core, nrow, hj):
    keep = jnp.where(core == 0, part[:, :hj], part[:, hj:])
    send = jnp.where(core == 0, part[:, hj:], part[:, :hj])
    got = lax.ppermute(send, "row", [(i, i ^ 1) for i in range(nrow)])
    return jnp.where(
        core == 0, jnp.concatenate([keep, got], axis=3), jnp.concatenate([got, keep], axis=3)
    )


def gather_amplitudes(t_part, cl):
    nrow = lax.axis_size("row")
    r = lax.axis_index("row")
    x = r // 4
    zh = (r // 2) % 2
    core = r % 2
    ng, nj, nk, ncc, nb = t_part.shape
    hj = nj // 2
    hg = ng // 2
    swap = [(i, i ^ 2) for i in range(nrow)]
    zh_lo = lax.ppermute(t_part[:hg], "row", swap)
    zh_hi = lax.ppermute(t_part[hg:], "row", swap)
    own = ring4_pieces(core_quad(t_part, core, nrow, hj), "row", nrow, 4)
    pos = x - cl
    mine = jnp.zeros((ng, hj, nk, 16 * ncc, nb), t_part.dtype)
    for step in (1, 2, 3, 0):
        piece = own[step]
        mine = lax.dynamic_update_slice_in_dim(
            mine, piece, ((pos - step) % 4) * 4 * ncc + zh * 2 * ncc, axis=3
        )
    for goff, zpart in ((0, zh_lo), (hg, zh_hi)):
        far = ring4_pieces(core_quad(zpart, core, nrow, hj), "row", nrow, 4)
        for step, piece in enumerate(far):
            mine = lax.dynamic_update_slice(
                mine, piece, (goff, 0, 0, ((pos - step) % 4) * 4 * ncc + (1 - zh) * 2 * ncc, 0)
            )
    other = lax.ppermute(mine, "row", [(i, i ^ 1) for i in range(nrow)])
    return mine, other


def gather_integrals(w_part):
    ng = w_part.shape[0]
    w = w_part
    fwd = shift_perm(4, 1, 1)
    bwd = shift_perm(4, -1, 1)
    from_left = lax.ppermute(w, "col", fwd)
    from_right = lax.ppermute(w, "col", bwd)
    half = ng // 2
    opp_lo = lax.ppermute(from_left[:half], "col", fwd)
    opp_hi = lax.ppermute(from_right[half:], "col", bwd)
    opp = jnp.concatenate([opp_lo, opp_hi], axis=0)
    return [w, from_right, opp, from_left]


def ring_reduce_scatter(part):
    n = lax.axis_size("rep")
    d = lax.axis_index("rep")
    width = part.shape[0] // n
    fwd = [(i, (i + 1) % n) for i in range(n)]

    def chunk(t):
        return lax.dynamic_slice_in_dim(part, (t % n) * width, width, axis=0)

    acc = chunk(d + n - 1)
    for step in range(1, n):
        acc = lax.ppermute(acc, "rep", fwd) + chunk(d + 2 * n - step - 1)
    return acc


def body(integrals, amplitudes, virt_count, occ_irrep):
    ngroup = integrals.shape[0]
    k_local = integrals.shape[2]
    c_local = integrals.shape[3]
    nvirt = integrals.shape[4]
    rep_index = lax.axis_index("rep")
    col_index = lax.axis_index("col")
    core = lax.axis_index("row") % 2
    occ_local = lax.dynamic_slice_in_dim(occ_irrep, rep_index * k_local, k_local)
    groups = jnp.arange(ngroup, dtype=jnp.int32)
    blocks = jnp.bitwise_xor(groups[:, None], occ_local[None, :])
    onehot = blocks[:, :, None] == groups[None, None, :]
    limit = jnp.sum(jnp.where(onehot, virt_count[None, None, :], 0), axis=2)
    c_global = col_index * c_local + jnp.arange(c_local, dtype=jnp.int32)
    c_live = c_global[None, None, :] < limit[:, :, None]
    places = jnp.arange(nvirt, dtype=jnp.int32)
    a_live = places[None, :] < virt_count[:, None]
    keep = c_live[:, None, :, :, None] & a_live[:, None, None, None, :]
    masked = jnp.where(keep, integrals, jnp.zeros_like(integrals))
    owned = ngroup // lax.axis_size("rep")
    w_blocks = gather_integrals(masked)
    t_mine, t_other = gather_amplitudes(amplitudes, col_index)
    sums = []
    for t_half, name in ((t_mine, "em"), (t_other, "eo")):
        width = c_local
        part = None
        for s, w_blk in enumerate(w_blocks):
            term = jnp.einsum(
                "gikca,gjkcb->giajb",
                w_blk,
                t_half[:, :, :, s * width:(s + 1) * width],
                preferred_element_type=jnp.float32,
            )
            part = term if part is None else part + term
        if name == "em":
            sums.append(ring_reduce_scatter(part))
        else:
            sums.append(lax.psum_scatter(part, "rep", scatter_dimension=0, tiled=True))
    summed = jnp.where(
        core == 0, jnp.concatenate(sums, axis=3), jnp.concatenate(sums[::-1], axis=3)
    )
    own_counts = lax.dynamic_slice_in_dim(virt_count, rep_index * owned, owned)
    b_live = places[None, :] < own_counts[:, None]
    result = jnp.where(b_live[:, None, None, None, :], summed, jnp.zeros_like(summed))
    return result.astype(jnp.bfloat16)


def solution(mesh):
    return jax.shard_map(
        body,
        mesh=mesh,
        in_specs=(P(None, "row", "rep", "col", None), P(None, "col", "rep", "row", None), P(), P()),
        out_specs=P("rep", "row", None, "col", None),
        check_vma=False,
    )
```

```python
import jax
import jax.numpy as jnp
from jax import lax
from jax.sharding import PartitionSpec as P


def shift_perm(n, step, period):
    pairs = []
    for i in range(n):
        pos = (i // period) % 4
        pairs.append((i, i + ((pos + step) % 4 - pos) * period))
    return pairs


def ring4_pieces(block, axis, n, period):
    fwd = shift_perm(n, 1, period)
    bwd = shift_perm(n, -1, period)
    from_left = lax.ppermute(block, axis, fwd)
    from_right = lax.ppermute(block, axis, bwd)
    half = block.shape[0] // 2
    opp_lo = lax.ppermute(from_left[:half], axis, fwd)
    opp_hi = lax.ppermute(from_right[half:], axis, bwd)
    opp = jnp.concatenate([opp_lo, opp_hi], axis=0)
    return [block, from_left, opp, from_right]


def core_quad(part, core, nrow, hj):
    keep = jnp.where(core == 0, part[:, :hj], part[:, hj:])
    send = jnp.where(core == 0, part[:, hj:], part[:, :hj])
    got = lax.ppermute(send, "row", [(i, i ^ 1) for i in range(nrow)])
    return jnp.where(
        core == 0, jnp.concatenate([keep, got], axis=3), jnp.concatenate([got, keep], axis=3)
    )


def gather_amplitudes(t_part, cl):
    nrow = lax.axis_size("row")
    r = lax.axis_index("row")
    x = r // 4
    zh = (r // 2) % 2
    core = r % 2
    ng, nj, nk, ncc, nb = t_part.shape
    hj = nj // 2
    hg = ng // 2
    swap = [(i, i ^ 2) for i in range(nrow)]
    zh_lo = lax.ppermute(t_part[:hg], "row", swap)
    zh_hi = lax.ppermute(t_part[hg:], "row", swap)
    own = ring4_pieces(core_quad(t_part, core, nrow, hj), "row", nrow, 4)
    pos = x - cl
    mine = jnp.zeros((ng, hj, nk, 16 * ncc, nb), t_part.dtype)
    for step in (1, 2, 3, 0):
        piece = own[step]
        mine = lax.dynamic_update_slice_in_dim(
            mine, piece, ((pos - step) % 4) * 4 * ncc + zh * 2 * ncc, axis=3
        )
    for goff, zpart in ((0, zh_lo), (hg, zh_hi)):
        far = ring4_pieces(core_quad(zpart, core, nrow, hj), "row", nrow, 4)
        for step, piece in enumerate(far):
            mine = lax.dynamic_update_slice(
                mine, piece, (goff, 0, 0, ((pos - step) % 4) * 4 * ncc + (1 - zh) * 2 * ncc, 0)
            )
    other = lax.ppermute(mine, "row", [(i, i ^ 1) for i in range(nrow)])
    return mine, other


def gather_integrals(w_part):
    ng = w_part.shape[0]
    w = w_part
    fwd = shift_perm(4, 1, 1)
    bwd = shift_perm(4, -1, 1)
    from_left = lax.ppermute(w, "col", fwd)
    from_right = lax.ppermute(w, "col", bwd)
    half = ng // 2
    opp_lo = lax.ppermute(from_left[:half], "col", fwd)
    opp_hi = lax.ppermute(from_right[half:], "col", bwd)
    opp = jnp.concatenate([opp_lo, opp_hi], axis=0)
    return [w, from_right, opp, from_left]


def ring_reduce_scatter(part, dirn, head):
    n = lax.axis_size("rep")
    d = lax.axis_index("rep")
    width = part.shape[0] // n
    perm = [(i, (i + dirn) % n) for i in range(n)]

    def chunk(t):
        return lax.dynamic_slice_in_dim(part, (t % n) * width, width, axis=0)

    acc = head
    for step in range(1, n):
        acc = lax.ppermute(acc, "rep", perm) + chunk(d + 2 * n - (step + 1) * dirn)
    return acc


def body(integrals, amplitudes, virt_count, occ_irrep):
    ngroup = integrals.shape[0]
    k_local = integrals.shape[2]
    c_local = integrals.shape[3]
    nvirt = integrals.shape[4]
    rep_index = lax.axis_index("rep")
    col_index = lax.axis_index("col")
    core = lax.axis_index("row") % 2
    occ_local = lax.dynamic_slice_in_dim(occ_irrep, rep_index * k_local, k_local)
    groups = jnp.arange(ngroup, dtype=jnp.int32)
    blocks = jnp.bitwise_xor(groups[:, None], occ_local[None, :])
    onehot = blocks[:, :, None] == groups[None, None, :]
    limit = jnp.sum(jnp.where(onehot, virt_count[None, None, :], 0), axis=2)
    c_global = col_index * c_local + jnp.arange(c_local, dtype=jnp.int32)
    c_live = c_global[None, None, :] < limit[:, :, None]
    places = jnp.arange(nvirt, dtype=jnp.int32)
    a_live = places[None, :] < virt_count[:, None]
    keep = c_live[:, None, :, :, None] & a_live[:, None, None, None, :]
    masked = jnp.where(keep, integrals, jnp.zeros_like(integrals))
    owned = ngroup // lax.axis_size("rep")
    w_blocks = gather_integrals(masked)
    t_mine, t_other = gather_amplitudes(amplitudes, col_index)
    nrep = lax.axis_size("rep")
    cw = ngroup // nrep
    width = c_local

    def dots(w_list, t_half):
        part = None
        for s, w_blk in enumerate(w_list):
            term = jnp.einsum(
                "gikca,gjkcb->giajb",
                w_blk,
                t_half[:, :, :, s * width:(s + 1) * width],
                preferred_element_type=jnp.float32,
            )
            part = term if part is None else part + term
        return part

    sums = []
    for t_half, dirn in ((t_mine, 1), (t_other, -1)):
        first = ((rep_index + nrep - dirn) % nrep) * cw
        head = dots(
            [lax.dynamic_slice_in_dim(w, first, cw, axis=0) for w in w_blocks],
            lax.dynamic_slice_in_dim(t_half, first, cw, axis=0),
        )
        part = dots(w_blocks, t_half)
        sums.append(ring_reduce_scatter(part, dirn, head))
    summed = jnp.where(
        core == 0, jnp.concatenate(sums, axis=3), jnp.concatenate(sums[::-1], axis=3)
    )
    own_counts = lax.dynamic_slice_in_dim(virt_count, rep_index * owned, owned)
    b_live = places[None, :] < own_counts[:, None]
    result = jnp.where(b_live[:, None, None, None, :], summed, jnp.zeros_like(summed))
    return result.astype(jnp.bfloat16)


def solution(mesh):
    return jax.shard_map(
        body,
        mesh=mesh,
        in_specs=(P(None, "row", "rep", "col", None), P(None, "col", "rep", "row", None), P(), P()),
        out_specs=P("rep", "row", None, "col", None),
        check_vma=False,
    )
```

```python
import jax
import jax.numpy as jnp
from jax import lax
from jax.sharding import PartitionSpec as P


def shift_perm(n, step, period):
    pairs = []
    for i in range(n):
        pos = (i // period) % 4
        pairs.append((i, i + ((pos + step) % 4 - pos) * period))
    return pairs


def ring4_pieces(block, axis, n, period):
    fwd = shift_perm(n, 1, period)
    bwd = shift_perm(n, -1, period)
    from_left = lax.ppermute(block, axis, fwd)
    from_right = lax.ppermute(block, axis, bwd)
    half = block.shape[0] // 2
    opp_lo = lax.ppermute(from_left[:half], axis, fwd)
    opp_hi = lax.ppermute(from_right[half:], axis, bwd)
    opp = jnp.concatenate([opp_lo, opp_hi], axis=0)
    return [block, from_left, opp, from_right]


def core_quad(part, core, nrow, hj):
    keep = jnp.where(core == 0, part[:, :hj], part[:, hj:])
    send = jnp.where(core == 0, part[:, hj:], part[:, :hj])
    got = lax.ppermute(send, "row", [(i, i ^ 1) for i in range(nrow)])
    return jnp.where(
        core == 0, jnp.concatenate([keep, got], axis=3), jnp.concatenate([got, keep], axis=3)
    )


def gather_amplitudes(t_part, cl):
    nrow = lax.axis_size("row")
    r = lax.axis_index("row")
    x = r // 4
    zh = (r // 2) % 2
    core = r % 2
    ng, nj, nk, ncc, nb = t_part.shape
    hj = nj // 2
    hg = ng // 2
    swap = [(i, i ^ 2) for i in range(nrow)]
    zh_lo = lax.ppermute(t_part[:hg], "row", swap)
    zh_hi = lax.ppermute(t_part[hg:], "row", swap)
    own = ring4_pieces(core_quad(t_part, core, nrow, hj), "row", nrow, 4)
    pos = x - cl
    mine = jnp.zeros((ng, hj, nk, 16 * ncc, nb), t_part.dtype)
    for step in (1, 2, 3, 0):
        piece = own[step]
        mine = lax.dynamic_update_slice_in_dim(
            mine, piece, ((pos - step) % 4) * 4 * ncc + zh * 2 * ncc, axis=3
        )
    halves = []
    for goff, zpart in ((0, zh_lo), (hg, zh_hi)):
        far = ring4_pieces(core_quad(zpart, core, nrow, hj), "row", nrow, 4)
        for step, piece in enumerate(far):
            mine = lax.dynamic_update_slice(
                mine, piece, (goff, 0, 0, ((pos - step) % 4) * 4 * ncc + (1 - zh) * 2 * ncc, 0)
            )
        halves.append(lax.ppermute(mine[goff:goff + hg], "row", [(i, i ^ 1) for i in range(nrow)]))
    other = jnp.concatenate(halves, axis=0)
    return mine, other


def gather_integrals(w_part):
    ng = w_part.shape[0]
    w = w_part
    fwd = shift_perm(4, 1, 1)
    bwd = shift_perm(4, -1, 1)
    from_left = lax.ppermute(w, "col", fwd)
    from_right = lax.ppermute(w, "col", bwd)
    half = ng // 2
    opp_lo = lax.ppermute(from_left[:half], "col", fwd)
    opp_hi = lax.ppermute(from_right[half:], "col", bwd)
    opp = jnp.concatenate([opp_lo, opp_hi], axis=0)
    return [w, from_right, opp, from_left]


def ring_reduce_scatter(part, dirn):
    n = lax.axis_size("rep")
    d = lax.axis_index("rep")
    width = part.shape[0] // n
    perm = [(i, (i + dirn) % n) for i in range(n)]

    def chunk(t):
        return lax.dynamic_slice_in_dim(part, (t % n) * width, width, axis=0)

    acc = chunk(d + n - dirn)
    for step in range(1, n):
        acc = lax.ppermute(acc, "rep", perm) + chunk(d + 2 * n - (step + 1) * dirn)
    return acc


def body(integrals, amplitudes, virt_count, occ_irrep):
    ngroup = integrals.shape[0]
    k_local = integrals.shape[2]
    c_local = integrals.shape[3]
    nvirt = integrals.shape[4]
    rep_index = lax.axis_index("rep")
    col_index = lax.axis_index("col")
    core = lax.axis_index("row") % 2
    occ_local = lax.dynamic_slice_in_dim(occ_irrep, rep_index * k_local, k_local)
    groups = jnp.arange(ngroup, dtype=jnp.int32)
    blocks = jnp.bitwise_xor(groups[:, None], occ_local[None, :])
    onehot = blocks[:, :, None] == groups[None, None, :]
    limit = jnp.sum(jnp.where(onehot, virt_count[None, None, :], 0), axis=2)
    c_global = col_index * c_local + jnp.arange(c_local, dtype=jnp.int32)
    c_live = c_global[None, None, :] < limit[:, :, None]
    places = jnp.arange(nvirt, dtype=jnp.int32)
    a_live = places[None, :] < virt_count[:, None]
    keep = c_live[:, None, :, :, None] & a_live[:, None, None, None, :]
    masked = jnp.where(keep, integrals, jnp.zeros_like(integrals))
    owned = ngroup // lax.axis_size("rep")
    w_blocks = gather_integrals(masked)
    t_mine, t_other = gather_amplitudes(amplitudes, col_index)
    sums = []
    for t_half, name in ((t_mine, "em"), (t_other, "eo")):
        width = c_local
        part = None
        for s, w_blk in enumerate(w_blocks):
            term = jnp.einsum(
                "gikca,gjkcb->giajb",
                w_blk,
                t_half[:, :, :, s * width:(s + 1) * width],
                preferred_element_type=jnp.float32,
            )
            part = term if part is None else part + term
        if name == "em":
            sums.append(ring_reduce_scatter(part, 1))
        else:
            sums.append(ring_reduce_scatter(part, -1))
    summed = jnp.where(
        core == 0, jnp.concatenate(sums, axis=3), jnp.concatenate(sums[::-1], axis=3)
    )
    own_counts = lax.dynamic_slice_in_dim(virt_count, rep_index * owned, owned)
    b_live = places[None, :] < own_counts[:, None]
    result = jnp.where(b_live[:, None, None, None, :], summed, jnp.zeros_like(summed))
    return result.astype(jnp.bfloat16)


def solution(mesh):
    return jax.shard_map(
        body,
        mesh=mesh,
        in_specs=(P(None, "row", "rep", "col", None), P(None, "col", "rep", "row", None), P(), P()),
        out_specs=P("rep", "row", None, "col", None),
        check_vma=False,
    )
```

```python
import jax
import jax.numpy as jnp
from jax import lax
from jax.sharding import PartitionSpec as P


def shift_perm(n, step, period):
    pairs = []
    for i in range(n):
        pos = (i // period) % 4
        pairs.append((i, i + ((pos + step) % 4 - pos) * period))
    return pairs


def ring4_pieces(block, axis, n, period):
    fwd = shift_perm(n, 1, period)
    bwd = shift_perm(n, -1, period)
    from_left = lax.ppermute(block, axis, fwd)
    from_right = lax.ppermute(block, axis, bwd)
    half = block.shape[0] // 2
    opp_lo = lax.ppermute(from_left[:half], axis, fwd)
    opp_hi = lax.ppermute(from_right[half:], axis, bwd)
    opp = jnp.concatenate([opp_lo, opp_hi], axis=0)
    return [block, from_left, opp, from_right]


def core_quad(part, core, nrow, hj):
    keep = jnp.where(core == 0, part[:, :hj], part[:, hj:])
    send = jnp.where(core == 0, part[:, hj:], part[:, :hj])
    got = lax.ppermute(send, "row", [(i, i ^ 1) for i in range(nrow)])
    return jnp.where(
        core == 0, jnp.concatenate([keep, got], axis=3), jnp.concatenate([got, keep], axis=3)
    )


def gather_amplitudes(t_part, cl):
    nrow = lax.axis_size("row")
    r = lax.axis_index("row")
    x = r // 4
    zh = (r // 2) % 2
    core = r % 2
    ng, nj, nk, ncc, nb = t_part.shape
    hj = nj // 2
    hg = ng // 2
    swap = [(i, i ^ 2) for i in range(nrow)]
    zh_lo = lax.ppermute(t_part[:hg], "row", swap)
    zh_hi = lax.ppermute(t_part[hg:], "row", swap)
    own = ring4_pieces(core_quad(t_part, core, nrow, hj), "row", nrow, 4)
    pos = x - cl
    mine = jnp.zeros((ng, hj, nk, 16 * ncc, nb), t_part.dtype)
    for step in (1, 2, 3, 0):
        piece = own[step]
        mine = lax.dynamic_update_slice_in_dim(
            mine, piece, ((pos - step) % 4) * 4 * ncc + zh * 2 * ncc, axis=3
        )
    for goff, zpart in ((0, zh_lo), (hg, zh_hi)):
        far = ring4_pieces(core_quad(zpart, core, nrow, hj), "row", nrow, 4)
        for step, piece in enumerate(far):
            mine = lax.dynamic_update_slice(
                mine, piece, (goff, 0, 0, ((pos - step) % 4) * 4 * ncc + (1 - zh) * 2 * ncc, 0)
            )
    other = lax.ppermute(mine, "row", [(i, i ^ 1) for i in range(nrow)])
    return mine, other


def gather_integrals(w_part):
    ng = w_part.shape[0]
    w = w_part
    fwd = shift_perm(4, 1, 1)
    bwd = shift_perm(4, -1, 1)
    from_left = lax.ppermute(w, "col", fwd)
    from_right = lax.ppermute(w, "col", bwd)
    half = ng // 2
    opp_lo = lax.ppermute(from_left[:half], "col", fwd)
    opp_hi = lax.ppermute(from_right[half:], "col", bwd)
    opp = jnp.concatenate([opp_lo, opp_hi], axis=0)
    return [w, from_right, opp, from_left]


def ring_reduce_scatter(part):
    n = lax.axis_size("rep")
    d = lax.axis_index("rep")
    width = part.shape[0] // n

    def chunk(t):
        return lax.dynamic_slice_in_dim(part, (t % n) * width, width, axis=0)

    got = []
    for step in range(1, n):
        got.append(lax.ppermute(chunk(d + step), "rep", [(i, (i + step) % n) for i in range(n)]))
    acc = chunk(d)
    for piece in got:
        acc = acc + piece
    return acc


def body(integrals, amplitudes, virt_count, occ_irrep):
    ngroup = integrals.shape[0]
    k_local = integrals.shape[2]
    c_local = integrals.shape[3]
    nvirt = integrals.shape[4]
    rep_index = lax.axis_index("rep")
    col_index = lax.axis_index("col")
    core = lax.axis_index("row") % 2
    occ_local = lax.dynamic_slice_in_dim(occ_irrep, rep_index * k_local, k_local)
    groups = jnp.arange(ngroup, dtype=jnp.int32)
    blocks = jnp.bitwise_xor(groups[:, None], occ_local[None, :])
    onehot = blocks[:, :, None] == groups[None, None, :]
    limit = jnp.sum(jnp.where(onehot, virt_count[None, None, :], 0), axis=2)
    c_global = col_index * c_local + jnp.arange(c_local, dtype=jnp.int32)
    c_live = c_global[None, None, :] < limit[:, :, None]
    places = jnp.arange(nvirt, dtype=jnp.int32)
    a_live = places[None, :] < virt_count[:, None]
    keep = c_live[:, None, :, :, None] & a_live[:, None, None, None, :]
    masked = jnp.where(keep, integrals, jnp.zeros_like(integrals))
    owned = ngroup // lax.axis_size("rep")
    w_blocks = gather_integrals(masked)
    t_mine, t_other = gather_amplitudes(amplitudes, col_index)
    sums = []
    for t_half in (t_mine, t_other):
        width = c_local
        part = None
        for s, w_blk in enumerate(w_blocks):
            term = jnp.einsum(
                "gikca,gjkcb->giajb",
                w_blk,
                t_half[:, :, :, s * width:(s + 1) * width],
                preferred_element_type=jnp.float32,
            )
            part = term if part is None else part + term
        sums.append(ring_reduce_scatter(part))
    summed = jnp.where(
        core == 0, jnp.concatenate(sums, axis=3), jnp.concatenate(sums[::-1], axis=3)
    )
    own_counts = lax.dynamic_slice_in_dim(virt_count, rep_index * owned, owned)
    b_live = places[None, :] < own_counts[:, None]
    result = jnp.where(b_live[:, None, None, None, :], summed, jnp.zeros_like(summed))
    return result.astype(jnp.bfloat16)


def solution(mesh):
    return jax.shard_map(
        body,
        mesh=mesh,
        in_specs=(P(None, "row", "rep", "col", None), P(None, "col", "rep", "row", None), P(), P()),
        out_specs=P("rep", "row", None, "col", None),
        check_vma=False,
    )
```
